512 devices in a mesh: grp: 16 (over x, y), clu: 32 (over z, core).
Axes of the slice: x: 4, y: 4, z: 16, core: 2. Of those that a mesh axis runs over, the one named last changes fastest.
Arguments:
- lower_inverse: bfloat16 [32, 2, 512, 512], P('clu', None, 'grp'), as said below
- upper_inverse: bfloat16 [32, 2, 512, 512], P('clu', None, 'grp'), as said below
- lower_factors: bfloat16 [32, 128, 2, 48, 512], P('clu', 'grp'), may hold values from -1.2578125 to 1.2578125
- upper_factors: bfloat16 [32, 128, 2, 48, 512], P('clu', 'grp'), may hold values from -1.2578125 to 1.2578125
- lower_ranks: int32 [32, 128], P('clu', 'grp'), may hold values from 16 to 48
- upper_ranks: int32 [32, 128], P('clu', 'grp'), may hold values from 16 to 48
- pivots: int32 [32, 512], P('clu'), may hold values from 0 to 511, each once within a row
- pair_lower: int32 [32, 512], P('clu', 'grp'), may hold values from 0 to 7
- pair_upper: int32 [32, 512], P('clu', 'grp'), may hold values from 0 to 7
- pair_owner: int32 [32, 512, 1], P('clu', 'grp'), may hold values from 0 to 31; in each aligned block of 32 rows (0 to 31, 32 to 63, ..., all dimensions but the last counted through in order) at most 2 rows name the same one
Outputs:
- lower_solved: bfloat16 [32, 128, 2, 48, 512], P('clu', 'grp')
- upper_solved: bfloat16 [32, 128, 2, 48, 512], P('clu', 'grp')
- arrived: bfloat16 [32, 16, 32, 2, 2, 2304], P('clu', 'grp')
The draws below stay inside these ranges and needn't reach their ends.
Inputs may be any that keep to these rules, and one draw needn't show every extreme that they name: `lower_inverse`: each cluster's matrix is unit lower triangular: zeros above the diagonal, one on the real part's diagonal and zero on the imaginary part's. `upper_inverse`: each cluster's matrix is upper triangular: zeros below the diagonal in both parts. `pair_owner`: among the 32 pairs of one share, at most 2 name the same owner, and some share reaches it.
All inputs are finite; a program needn't handle non-finite values.
Results may differ from the reference program's by a relative error of at most 0.0058.
Values may be sent and summed in bfloat16 or wider, within the bound.
No kernel may reach another device: no remote copies, remote signals or barrier semaphores. Data moves between devices by JAX's collectives and lax.ppermute only.
A program may use at most 64 MiB of HBM per device.

```python
import math
import jax
import jax.numpy as jnp
import numpy as np
from jax import lax

B = 512
R = 48
BLK_DEV = 8
SEND_CAP = 2
PAIRS_DEV = 32
BLOCKS = 128
PAIRS = 512
N_GRP = 16
N_CLU = 32


def off_diagonal(key, shape):
    keys = jax.random.split(key, 1)
    random_part = jax.random.normal(keys[0], shape, jnp.float32)
    return random_part * (0.8 / math.sqrt(B))


def draw_lower_inverse(key, part):
    shape = (N_CLU, 2, B, B)
    row_index = lax.broadcasted_iota(jnp.int32, shape, 2)
    column_index = lax.broadcasted_iota(jnp.int32, shape, 3)
    component = lax.broadcasted_iota(jnp.int32, shape, 1)
    random_part = off_diagonal(jax.random.fold_in(key, 11), shape)
    diagonal_ones = jnp.where((row_index == column_index) & (component == 0), 1.0, 0.0)
    return (jnp.where(column_index < row_index, random_part, 0.0) + diagonal_ones).astype(jnp.bfloat16)


def draw_upper_inverse(key, part):
    shape = (N_CLU, 2, B, B)
    row_index = lax.broadcasted_iota(jnp.int32, shape, 2)
    column_index = lax.broadcasted_iota(jnp.int32, shape, 3)
    component = lax.broadcasted_iota(jnp.int32, shape, 1)
    keys = jax.random.split(jax.random.fold_in(key, 23), 3)
    random_part = off_diagonal(keys[0], shape)
    magnitude = jnp.exp(jax.random.uniform(keys[1], shape, jnp.float32, math.log(0.5), math.log(2.0)))
    phase_part = 0.3 * jax.random.normal(keys[2], shape, jnp.float32)
    diagonal_values = jnp.where(component == 0, magnitude, phase_part)
    upper_part = jnp.where(column_index > row_index, random_part, jnp.where(column_index == row_index, diagonal_values, 0.0))
    return upper_part.astype(jnp.bfloat16)


def touch_ends(array, key, smallest, high):
    longest = array.shape.index(max(array.shape))
    spots = []
    for shift in (0, 1):
        where = [jax.random.randint(jax.random.fold_in(key, axis), (), 0, length) for axis, length in enumerate(array.shape)]
        where[longest] = (where[longest] + shift) % array.shape[longest]
        spots.append(tuple(where))
    return array.at[spots[0]].set(smallest).at[spots[1]].set(high)


def level_of(own_key, extent, cuts, least, high):
    level, own = 1.0, jax.random.fold_in(own_key, 6)
    for axis_at, blocks in cuts:
        steps = jnp.exp(jax.random.uniform(jax.random.fold_in(own, axis_at), (blocks,), jnp.float32, least / len(cuts), high / len(cuts)))
        level = level * jnp.repeat(steps, extent[axis_at] // blocks).reshape([-1 if axis == axis_at else 1 for axis in range(len(extent))])
    return level


def deal_out(key, own, number, rows, number_of, top, most, lean):
    ranking = jax.random.permutation(key, number_of)
    heavy_load, usual = shares(number_of, rows * top, most, lean, True), shares(number_of, rows * top, most, lean, False)
    places = jnp.arange(number_of)

    def named(lengths, rotation):
        used = int((lengths > 0).sum())
        fixed = max(1, used // 4)
        moved = fixed + (places - fixed + rotation * (used - fixed)) % max(1, number_of - fixed)
        return jnp.zeros((number_of,), jnp.int32).at[ranking[jnp.where(places < fixed, places, moved)]].set(jnp.asarray(lengths, jnp.int32))

    lengths = jnp.where(number % 4 == 0, named(heavy_load, number // 4), named(usual, number - number // 4 - 1))
    mixed = jax.random.permutation(jax.random.fold_in(own, 3), number_of)
    source_of, sink = mixed[0:number_of // 2 * 2:2], mixed[1:number_of // 2 * 2:2]
    room = jnp.minimum(lengths[source_of] - 1, most - lengths[sink]) // 2
    room = jnp.where((source_of == ranking[0]) | (sink == ranking[0]) | (lengths[sink] == 0), 0, jnp.maximum(room, 0))
    moved = jax.random.randint(jax.random.fold_in(own, 4), (number_of // 2,), 0, 1 << 20) % (room + 1)
    lengths = lengths.at[source_of].add(-moved).at[sink].add(moved)
    items = jnp.searchsorted(jnp.cumsum(lengths), jnp.arange(rows * top), side="right").astype(jnp.int32)
    grid = items.reshape(top, rows).T
    grid = grid[jax.random.permutation(jax.random.fold_in(own, 1), rows)]
    rotation = jax.random.randint(jax.random.fold_in(own, 2), (rows, 1), 0, top)
    return jnp.take_along_axis(grid, (jnp.arange(top)[None, :] + rotation) % top, axis=1)


def shares(number_of, total, reach, skew, full):
    loads = [(1 << 20) // math.isqrt(standing ** skew) + 1 for standing in range(1, number_of + 1)]
    largest = reach if full else min(reach, max(-(-total // number_of), total * loads[0] // sum(loads)))
    least = 1 if total - largest >= number_of - 1 else 0
    counts, surplus = [largest] + [least] * (number_of - 1), total - largest - least * (number_of - 1)
    while surplus > 0:
        movable = [i for i in range(1, number_of) if counts[i] < largest] or [i for i in range(1, number_of) if counts[i] < reach]
        pool, left = sum([loads[i] for i in movable]), surplus
        for i in movable:
            extra = min(reach - counts[i], max(1, left * loads[i] // pool), surplus)
            counts[i] = counts[i] + extra
            surplus = surplus - extra
    return np.array(counts)


def noise(rng, dims, width, limit, cuts=(), kind=jnp.bfloat16):
    values = width * jax.random.normal(rng, dims, jnp.float32)
    if cuts:
        values = values * level_of(rng, dims, cuts, -0.22, 0.18)
    return jnp.clip(values, -limit, limit).astype(kind)


def setup_inputs(seed: int = 0) -> dict:
    arg_keys = jax.random.split(jax.random.key(seed), 11)
    lower_inverse = draw_lower_inverse(jax.random.fold_in(arg_keys[10], 71), 0)
    upper_inverse = draw_upper_inverse(jax.random.fold_in(arg_keys[10], 71), 0)
    lower_factors = noise(arg_keys[2], (N_CLU, BLOCKS, 2, R, B), (B ** -0.25), 1.2578125, ((0, 32), (1, 16)))
    upper_factors = noise(arg_keys[3], (N_CLU, BLOCKS, 2, R, B), (B ** -0.25), 1.2578125, ((0, 32), (1, 16)))
    lower_ranks = touch_ends(jax.random.randint(arg_keys[4], (N_CLU, BLOCKS), R // 3, R + 1), jax.random.fold_in(arg_keys[4], 1), R // 3, R).astype(jnp.int32)
    upper_ranks = touch_ends(jax.random.randint(arg_keys[5], (N_CLU, BLOCKS), R // 3, R + 1), jax.random.fold_in(arg_keys[5], 1), R // 3, R).astype(jnp.int32)
    pivots = jax.vmap(lambda own: jax.random.permutation(own, B))(jax.random.split(arg_keys[6], N_CLU)).reshape((N_CLU, B)).astype(jnp.int32)
    pair_lower = touch_ends(jax.random.randint(arg_keys[7], (N_CLU, PAIRS), 0, BLK_DEV), jax.random.fold_in(arg_keys[7], 1), 0, BLK_DEV - 1).astype(jnp.int32)
    pair_upper = touch_ends(jax.random.randint(arg_keys[8], (N_CLU, PAIRS), 0, BLK_DEV), jax.random.fold_in(arg_keys[8], 1), 0, BLK_DEV - 1).astype(jnp.int32)
    pair_owner_keys = jax.random.split(jax.random.fold_in(arg_keys[9], 1), N_CLU * PAIRS // PAIRS_DEV)
    pair_owner_turns = jax.random.permutation(jax.random.fold_in(arg_keys[9], 3), N_CLU * PAIRS // PAIRS_DEV)
    pair_owner = jax.vmap(lambda own, number: deal_out(jax.random.fold_in(arg_keys[9], 2), own, number, PAIRS_DEV, N_CLU, 1, SEND_CAP, 2))(pair_owner_keys, pair_owner_turns).reshape((N_CLU, PAIRS, 1))
    return {"lower_inverse": lower_inverse, "upper_inverse": upper_inverse, "lower_factors": lower_factors, "upper_factors": upper_factors, "lower_ranks": lower_ranks, "upper_ranks": upper_ranks, "pivots": pivots, "pair_lower": pair_lower, "pair_upper": pair_upper, "pair_owner": pair_owner}


def solve_side(factors, matrix):
    block_count = factors.shape[0]
    left_real = factors[:, 0].reshape(block_count * R, B).astype(jnp.float32)
    left_imag = factors[:, 1].reshape(block_count * R, B).astype(jnp.float32)
    right_real = matrix[0].astype(jnp.float32)
    right_imag = matrix[1].astype(jnp.float32)
    real_part = jnp.dot(left_real, right_real, preferred_element_type=jnp.float32) - jnp.dot(left_imag, right_imag, preferred_element_type=jnp.float32)
    imag_part = jnp.dot(left_real, right_imag, preferred_element_type=jnp.float32) + jnp.dot(left_imag, right_real, preferred_element_type=jnp.float32)
    result = jnp.stack([real_part, imag_part], 0).reshape(2, block_count, R, B)
    return jnp.transpose(result, (1, 0, 2, 3)).astype(jnp.bfloat16)


def mask_rows(factors, block_ranks):
    row_index = lax.broadcasted_iota(jnp.int32, (factors.shape[0], R), 1)
    row_mask = row_index < block_ranks[:, None]
    return jnp.where(row_mask[:, None, :, None], factors, jnp.zeros((), factors.dtype))


def product(left, right):
    return jnp.einsum("prb,psb->prs", left, right)


def one_cluster(inputs):
    lower_inv, upper_inv, lower_fac, upper_fac, lower_rk, upper_rk, pivot_order, pick_lower, pick_upper, owners = inputs
    lower_masked = mask_rows(lower_fac, lower_rk)
    upper_masked = mask_rows(upper_fac, upper_rk)
    upper_pivoted = jnp.take(upper_masked, pivot_order.astype(jnp.int32), axis=3)
    lower_out = solve_side(lower_masked, upper_inv)
    upper_out = solve_side(upper_pivoted, jnp.swapaxes(lower_inv, 1, 2))
    pair_ids = jnp.arange(PAIRS, dtype=jnp.int32)
    share_ids = pair_ids // PAIRS_DEV
    lower_pick = (share_ids * BLK_DEV + pick_lower).astype(jnp.int32)
    upper_pick = (share_ids * BLK_DEV + pick_upper).astype(jnp.int32)
    left_blocks = lower_out[lower_pick].astype(jnp.float32)
    right_blocks = upper_out[upper_pick].astype(jnp.float32)
    real_part = product(left_blocks[:, 0], right_blocks[:, 0]) - product(left_blocks[:, 1], right_blocks[:, 1])
    imag_part = product(left_blocks[:, 0], right_blocks[:, 1]) + product(left_blocks[:, 1], right_blocks[:, 0])
    cores = jnp.stack([real_part, imag_part], 1).reshape(PAIRS, 2, R * R).astype(jnp.bfloat16)
    owner_ids = owners[:, 0]
    same_owner = (share_ids[:, None] == share_ids[None, :]) & (owner_ids[:, None] == owner_ids[None, :]) & (pair_ids[None, :] < pair_ids[:, None])
    slots = jnp.sum(same_owner.astype(jnp.int32), axis=1).astype(jnp.int32)
    return lower_out, upper_out, cores, owner_ids.astype(jnp.int32), slots


def reference(lower_inverse, upper_inverse, lower_factors, upper_factors, lower_ranks, upper_ranks, pivots, pair_lower, pair_upper, pair_owner):
    lower_solved, upper_solved, cores, owner_all, slot_all = lax.map(one_cluster, (lower_inverse, upper_inverse, lower_factors, upper_factors, lower_ranks, upper_ranks, pivots, pair_lower, pair_upper, pair_owner))
    pair_ids = jnp.arange(PAIRS, dtype=jnp.int32)
    share_all = jnp.broadcast_to((pair_ids // PAIRS_DEV)[None, :], (N_CLU, PAIRS)).astype(jnp.int32)
    cluster_all = jnp.broadcast_to(jnp.arange(N_CLU, dtype=jnp.int32)[:, None], (N_CLU, PAIRS)).astype(jnp.int32)
    arrived = jnp.zeros((N_CLU, N_GRP, N_CLU, SEND_CAP, 2, R * R), jnp.bfloat16)
    arrived = arrived.at[owner_all, share_all, cluster_all, slot_all].set(cores)
    return lower_solved, upper_solved, arrived
```

```python
import jax
import jax.numpy as jnp
from jax import lax
from jax.sharding import PartitionSpec as P

SEND_CAP = 2


def mask_rows(factors, block_ranks):
    rank_width = factors.shape[2]
    row_index = lax.broadcasted_iota(jnp.int32, (factors.shape[0], rank_width), 1)
    row_mask = row_index < block_ranks[:, None]
    return jnp.where(row_mask[:, None, :, None], factors, jnp.zeros((), factors.dtype))


def product(left, right):
    return jnp.einsum("prb,psb->prs", left, right, preferred_element_type=jnp.float32)


def gather_inverses(lower_rows, upper_rows):
    groups = lax.axis_size("grp")
    rows = lower_rows.shape[1]
    width = lower_rows.shape[2]
    span = width + rows
    start = lax.axis_index("grp") * rows
    both = jnp.concatenate([upper_rows, lower_rows], axis=-1)
    packed = lax.dynamic_slice_in_dim(both, start, span, axis=2)
    copies = jnp.broadcast_to(packed[None], (groups,) + packed.shape)
    blocks = lax.all_to_all(copies, "grp", split_axis=0, concat_axis=0, tiled=True)
    upper_blocks, lower_blocks = [], []
    for source in range(groups):
        block = blocks[source]
        cut = width - source * rows
        upper_blocks.append(jnp.pad(block[..., :cut], ((0, 0), (0, 0), (source * rows, 0))))
        lower_blocks.append(jnp.pad(block[..., cut:], ((0, 0), (0, 0), (0, cut - rows))))
    return jnp.concatenate(lower_blocks, axis=1), jnp.concatenate(upper_blocks, axis=1)


def per_device(
    lower_inverse,
    upper_inverse,
    lower_factors,
    upper_factors,
    lower_ranks,
    upper_ranks,
    pivots,
    pair_lower,
    pair_upper,
    pair_owner,
):
    lower_masked = mask_rows(lower_factors[0], lower_ranks[0])
    upper_masked = mask_rows(upper_factors[0], upper_ranks[0])
    upper_pivoted = jnp.take(upper_masked, pivots[0], axis=3)
    block_count = lower_masked.shape[0]
    rank_width = lower_masked.shape[2]
    panel_count = lower_masked.shape[3]
    lower_real = lower_masked[:, 0].reshape(block_count * rank_width, panel_count)
    lower_imag = lower_masked[:, 1].reshape(block_count * rank_width, panel_count)
    upper_real = upper_pivoted[:, 0].reshape(block_count * rank_width, panel_count)
    upper_imag = upper_pivoted[:, 1].reshape(block_count * rank_width, panel_count)
    contract_last = (((1,), (1,)), ((), ()))
    lower_piece, upper_piece = gather_inverses(lower_inverse[0], upper_inverse[0])
    piece_real = upper_piece[0]
    piece_imag = upper_piece[1]
    real_part = jnp.dot(lower_real, piece_real, preferred_element_type=jnp.float32) - jnp.dot(
        lower_imag, piece_imag, preferred_element_type=jnp.float32
    )
    imag_part = jnp.dot(lower_real, piece_imag, preferred_element_type=jnp.float32) + jnp.dot(
        lower_imag, piece_real, preferred_element_type=jnp.float32
    )
    lower_totals = jnp.stack([real_part, imag_part], 0)
    piece_real = lower_piece[0]
    piece_imag = lower_piece[1]
    real_part = lax.dot_general(
        upper_real, piece_real, contract_last, preferred_element_type=jnp.float32
    ) - lax.dot_general(upper_imag, piece_imag, contract_last, preferred_element_type=jnp.float32)
    imag_part = lax.dot_general(
        upper_real, piece_imag, contract_last, preferred_element_type=jnp.float32
    ) + lax.dot_general(upper_imag, piece_real, contract_last, preferred_element_type=jnp.float32)
    upper_totals = jnp.stack([real_part, imag_part], 0)
    lower_solved = jnp.transpose(
        lower_totals.astype(jnp.bfloat16).reshape(2, block_count, rank_width, panel_count),
        (1, 0, 2, 3),
    )
    upper_solved = jnp.transpose(
        upper_totals.astype(jnp.bfloat16).reshape(2, block_count, rank_width, panel_count),
        (1, 0, 2, 3),
    )
    left_blocks = lower_solved[pair_lower[0]]
    right_blocks = upper_solved[pair_upper[0]]
    pair_count = left_blocks.shape[0]
    real_part = product(left_blocks[:, 0], right_blocks[:, 0]) - product(
        left_blocks[:, 1], right_blocks[:, 1]
    )
    imag_part = product(left_blocks[:, 0], right_blocks[:, 1]) + product(
        left_blocks[:, 1], right_blocks[:, 0]
    )
    cores = (
        jnp.stack([real_part, imag_part], 1)
        .reshape(pair_count, 2 * rank_width * rank_width)
        .astype(jnp.bfloat16)
    )
    owners = pair_owner[0, :, 0]
    pair_ids = lax.broadcasted_iota(jnp.int32, (pair_count,), 0)
    same_owner = (owners[:, None] == owners[None, :]) & (pair_ids[None, :] < pair_ids[:, None])
    slots = jnp.sum(same_owner.astype(jnp.int32), axis=1)
    clusters = lax.axis_size("clu")
    target_slot = owners * SEND_CAP + slots
    slot_ids = lax.broadcasted_iota(jnp.int32, (clusters * SEND_CAP, pair_count), 0)
    one_hot = (slot_ids == target_slot[None, :]).astype(jnp.bfloat16)
    buffer = jnp.dot(one_hot, cores, preferred_element_type=jnp.float32).astype(jnp.bfloat16)
    buffer = buffer.reshape(clusters, SEND_CAP, 2, rank_width * rank_width)
    arrived = lax.all_to_all(buffer, "clu", split_axis=0, concat_axis=0, tiled=True)
    return (lower_solved[None], upper_solved[None], arrived[None, None])


def solution(mesh):
    in_specs = (
        P("clu", None, "grp", None),
        P("clu", None, "grp", None),
        P("clu", "grp", None, None, None),
        P("clu", "grp", None, None, None),
        P("clu", "grp"),
        P("clu", "grp"),
        P("clu", None),
        P("clu", "grp"),
        P("clu", "grp"),
        P("clu", "grp", None),
    )
    out_specs = (
        P("clu", "grp", None, None, None),
        P("clu", "grp", None, None, None),
        P("clu", "grp", None, None, None, None),
    )
    return jax.shard_map(
        per_device, mesh=mesh, in_specs=in_specs, out_specs=out_specs, check_vma=False
    )
```

```python
import jax
import jax.numpy as jnp
from jax import lax
from jax.sharding import PartitionSpec as P

SEND_CAP = 2


def mask_rows(factors, block_ranks):
    rank_width = factors.shape[2]
    row_index = lax.broadcasted_iota(jnp.int32, (factors.shape[0], rank_width), 1)
    row_mask = row_index < block_ranks[:, None]
    return jnp.where(row_mask[:, None, :, None], factors, jnp.zeros((), factors.dtype))


def product(left, right):
    return jnp.einsum("prb,psb->prs", left, right, preferred_element_type=jnp.float32)


def gather_inverses(lower_rows, upper_rows):
    groups = lax.axis_size("grp")
    rows = lower_rows.shape[1]
    width = lower_rows.shape[2]
    span = width + rows
    start = lax.axis_index("grp") * rows
    both = jnp.concatenate([upper_rows, lower_rows], axis=-1)
    packed = lax.dynamic_slice_in_dim(both, start, span, axis=2)
    copies = jnp.broadcast_to(packed[None], (groups,) + packed.shape)
    blocks = lax.all_to_all(copies, "grp", split_axis=0, concat_axis=0, tiled=True)
    upper_blocks, lower_blocks = [], []
    for source in range(groups):
        block = blocks[source]
        cut = width - source * rows
        upper_blocks.append(jnp.pad(block[..., :cut], ((0, 0), (0, 0), (source * rows, 0))))
        lower_blocks.append(jnp.pad(block[..., cut:], ((0, 0), (0, 0), (0, cut - rows))))
    return jnp.concatenate(lower_blocks, axis=1), jnp.concatenate(upper_blocks, axis=1)


def solve_rows(rows, right, contract):
    block_count, _, rank_width, panel_count = rows.shape
    flat = rows.reshape(block_count * 2 * rank_width, panel_count)
    totals = lax.dot_general(flat, right, contract, preferred_element_type=jnp.float32)
    totals = totals.reshape(block_count, 2, rank_width, 2 * panel_count)
    real_part = totals[:, 0, :, :panel_count] - totals[:, 1, :, panel_count:]
    imag_part = totals[:, 0, :, panel_count:] + totals[:, 1, :, :panel_count]
    return jnp.stack([real_part, imag_part], 1).astype(jnp.bfloat16)


def per_device(
    lower_inverse,
    upper_inverse,
    lower_factors,
    upper_factors,
    lower_ranks,
    upper_ranks,
    pivots,
    pair_lower,
    pair_upper,
    pair_owner,
):
    lower_masked = mask_rows(lower_factors[0], lower_ranks[0])
    upper_masked = mask_rows(upper_factors[0], upper_ranks[0])
    block_count, _, rank_width, panel_count = lower_masked.shape
    panel_ids = lax.broadcasted_iota(jnp.int32, (panel_count, panel_count), 0)
    pivot_matrix = (panel_ids == pivots[0][None, :]).astype(jnp.bfloat16)
    upper_pivoted = jnp.dot(
        upper_masked.reshape(-1, panel_count), pivot_matrix, preferred_element_type=jnp.float32
    ).astype(jnp.bfloat16).reshape(upper_masked.shape)
    lower_piece, upper_piece = gather_inverses(lower_inverse[0], upper_inverse[0])
    contract_first = (((1,), (0,)), ((), ()))
    contract_last = (((1,), (1,)), ((), ()))
    upper_right = jnp.concatenate([upper_piece[0], upper_piece[1]], axis=1)
    lower_right = jnp.concatenate([lower_piece[0], lower_piece[1]], axis=0)
    lower_solved = solve_rows(lower_masked, upper_right, contract_first)
    upper_solved = solve_rows(upper_pivoted, lower_right, contract_last)
    side = block_count * 2 * rank_width
    grams = lax.dot_general(
        lower_solved.reshape(side, panel_count),
        upper_solved.reshape(side, panel_count),
        contract_last,
        preferred_element_type=jnp.float32,
    ).reshape(block_count, 2, rank_width, block_count, 2, rank_width)
    real_part = grams[:, 0, :, :, 0, :] - grams[:, 1, :, :, 1, :]
    imag_part = grams[:, 0, :, :, 1, :] + grams[:, 1, :, :, 0, :]
    all_cores = (
        jnp.transpose(jnp.stack([real_part, imag_part], 0), (1, 3, 0, 2, 4))
        .reshape(block_count * block_count, 2 * rank_width * rank_width)
        .astype(jnp.bfloat16)
    )
    owners = pair_owner[0, :, 0]
    pair_count = owners.shape[0]
    pair_ids = lax.broadcasted_iota(jnp.int32, (pair_count,), 0)
    same_owner = (owners[:, None] == owners[None, :]) & (pair_ids[None, :] < pair_ids[:, None])
    slots = jnp.sum(same_owner.astype(jnp.int32), axis=1)
    clusters = lax.axis_size("clu")
    target_slot = owners * SEND_CAP + slots
    slot_ids = lax.broadcasted_iota(jnp.int32, (clusters * SEND_CAP, pair_count), 0)
    one_hot = (slot_ids == target_slot[None, :]).astype(jnp.float32)
    pair_block = pair_lower[0] * block_count + pair_upper[0]
    block_ids = lax.broadcasted_iota(jnp.int32, (pair_count, block_count * block_count), 1)
    pick = (block_ids == pair_block[:, None]).astype(jnp.float32)
    chooser = jnp.dot(one_hot, pick, preferred_element_type=jnp.float32).astype(jnp.bfloat16)
    buffer = jnp.dot(chooser, all_cores, preferred_element_type=jnp.float32).astype(jnp.bfloat16)
    buffer = buffer.reshape(clusters, SEND_CAP, 2, rank_width * rank_width)
    arrived = lax.all_to_all(buffer, "clu", split_axis=0, concat_axis=0, tiled=True)
    return (lower_solved[None], upper_solved[None], arrived[None, None])


def solution(mesh):
    in_specs = (
        P("clu", None, "grp", None),
        P("clu", None, "grp", None),
        P("clu", "grp", None, None, None),
        P("clu", "grp", None, None, None),
        P("clu", "grp"),
        P("clu", "grp"),
        P("clu", None),
        P("clu", "grp"),
        P("clu", "grp"),
        P("clu", "grp", None),
    )
    out_specs = (
        P("clu", "grp", None, None, None),
        P("clu", "grp", None, None, None),
        P("clu", "grp", None, None, None, None),
    )
    return jax.shard_map(
        per_device, mesh=mesh, in_specs=in_specs, out_specs=out_specs, check_vma=False
    )
```

```python
import jax
import jax.numpy as jnp
from jax import lax
from jax.sharding import PartitionSpec as P

SEND_CAP = 2


def mask_rows(factors, block_ranks):
    rank_width = factors.shape[2]
    row_index = lax.broadcasted_iota(jnp.int32, (factors.shape[0], rank_width), 1)
    row_mask = row_index < block_ranks[:, None]
    return jnp.where(row_mask[:, None, :, None], factors, jnp.zeros((), factors.dtype))


def product(left, right):
    return jnp.einsum("prb,psb->prs", left, right, preferred_element_type=jnp.float32)


def gather_inverses(lower_rows, upper_rows):
    groups = lax.axis_size("grp")
    rows = lower_rows.shape[1]
    width = lower_rows.shape[2]
    span = width + rows
    start = lax.axis_index("grp") * rows
    both = jnp.concatenate([upper_rows, lower_rows], axis=-1)
    packed = lax.dynamic_slice_in_dim(both, start, span, axis=2)
    copies = jnp.broadcast_to(packed[None], (groups,) + packed.shape)
    blocks = lax.all_to_all(copies, "grp", split_axis=0, concat_axis=0, tiled=True)
    upper_blocks, lower_blocks = [], []
    for source in range(groups):
        block = blocks[source]
        cut = width - source * rows
        upper_blocks.append(jnp.pad(block[..., :cut], ((0, 0), (0, 0), (source * rows, 0))))
        lower_blocks.append(jnp.pad(block[..., cut:], ((0, 0), (0, 0), (0, cut - rows))))
    return jnp.concatenate(lower_blocks, axis=1), jnp.concatenate(upper_blocks, axis=1)


def per_device(
    lower_inverse,
    upper_inverse,
    lower_factors,
    upper_factors,
    lower_ranks,
    upper_ranks,
    pivots,
    pair_lower,
    pair_upper,
    pair_owner,
):
    lower_masked = mask_rows(lower_factors[0], lower_ranks[0])
    upper_masked = mask_rows(upper_factors[0], upper_ranks[0])
    upper_pivoted = jnp.take(upper_masked, pivots[0], axis=3)
    block_count = lower_masked.shape[0]
    rank_width = lower_masked.shape[2]
    panel_count = lower_masked.shape[3]
    lower_real = lower_masked[:, 0].reshape(block_count * rank_width, panel_count)
    lower_imag = lower_masked[:, 1].reshape(block_count * rank_width, panel_count)
    upper_real = upper_pivoted[:, 0].reshape(block_count * rank_width, panel_count)
    upper_imag = upper_pivoted[:, 1].reshape(block_count * rank_width, panel_count)
    contract_last = (((1,), (1,)), ((), ()))
    lower_piece, upper_piece = gather_inverses(lower_inverse[0], upper_inverse[0])
    piece_real = upper_piece[0]
    piece_imag = upper_piece[1]
    real_part = jnp.dot(lower_real, piece_real, preferred_element_type=jnp.float32) - jnp.dot(
        lower_imag, piece_imag, preferred_element_type=jnp.float32
    )
    imag_part = jnp.dot(lower_real, piece_imag, preferred_element_type=jnp.float32) + jnp.dot(
        lower_imag, piece_real, preferred_element_type=jnp.float32
    )
    lower_totals = jnp.stack([real_part, imag_part], 0)
    piece_real = lower_piece[0]
    piece_imag = lower_piece[1]
    real_part = lax.dot_general(
        upper_real, piece_real, contract_last, preferred_element_type=jnp.float32
    ) - lax.dot_general(upper_imag, piece_imag, contract_last, preferred_element_type=jnp.float32)
    imag_part = lax.dot_general(
        upper_real, piece_imag, contract_last, preferred_element_type=jnp.float32
    ) + lax.dot_general(upper_imag, piece_real, contract_last, preferred_element_type=jnp.float32)
    upper_totals = jnp.stack([real_part, imag_part], 0)
    lower_totals = lower_totals.astype(jnp.bfloat16)
    upper_totals = upper_totals.astype(jnp.bfloat16)
    lower_solved = jnp.transpose(
        lower_totals.reshape(2, block_count, rank_width, panel_count), (1, 0, 2, 3)
    )
    upper_solved = jnp.transpose(
        upper_totals.reshape(2, block_count, rank_width, panel_count), (1, 0, 2, 3)
    )
    real_part = lax.dot_general(
        lower_totals[0], upper_totals[0], contract_last, preferred_element_type=jnp.float32
    ) - lax.dot_general(lower_totals[1], upper_totals[1], contract_last, preferred_element_type=jnp.float32)
    imag_part = lax.dot_general(
        lower_totals[0], upper_totals[1], contract_last, preferred_element_type=jnp.float32
    ) + lax.dot_general(lower_totals[1], upper_totals[0], contract_last, preferred_element_type=jnp.float32)
    grid = jnp.stack([real_part, imag_part], 0).reshape(2, block_count, rank_width, block_count, rank_width)
    grid = jnp.transpose(grid, (1, 3, 0, 2, 4)).reshape(
        block_count * block_count, 2, rank_width, rank_width
    )
    pair_count = pair_lower.shape[1]
    picked = jnp.take(grid, pair_lower[0] * block_count + pair_upper[0], axis=0)
    cores = picked.reshape(pair_count, 2 * rank_width * rank_width).astype(jnp.bfloat16)
    owners = pair_owner[0, :, 0]
    pair_ids = lax.broadcasted_iota(jnp.int32, (pair_count,), 0)
    same_owner = (owners[:, None] == owners[None, :]) & (pair_ids[None, :] < pair_ids[:, None])
    slots = jnp.sum(same_owner.astype(jnp.int32), axis=1)
    clusters = lax.axis_size("clu")
    target_slot = owners * SEND_CAP + slots
    slot_ids = lax.broadcasted_iota(jnp.int32, (clusters * SEND_CAP, pair_count), 0)
    one_hot = (slot_ids == target_slot[None, :]).astype(jnp.bfloat16)
    buffer = jnp.dot(one_hot, cores, preferred_element_type=jnp.float32).astype(jnp.bfloat16)
    buffer = buffer.reshape(clusters, SEND_CAP, 2, rank_width * rank_width)
    arrived = lax.all_to_all(buffer, "clu", split_axis=0, concat_axis=0, tiled=True)
    return (lower_solved[None], upper_solved[None], arrived[None, None])


def solution(mesh):
    in_specs = (
        P("clu", None, "grp", None),
        P("clu", None, "grp", None),
        P("clu", "grp", None, None, None),
        P("clu", "grp", None, None, None),
        P("clu", "grp"),
        P("clu", "grp"),
        P("clu", None),
        P("clu", "grp"),
        P("clu", "grp"),
        P("clu", "grp", None),
    )
    out_specs = (
        P("clu", "grp", None, None, None),
        P("clu", "grp", None, None, None),
        P("clu", "grp", None, None, None, None),
    )
    return jax.shard_map(
        per_device, mesh=mesh, in_specs=in_specs, out_specs=out_specs, check_vma=False
    )
```

```python
import jax
import jax.numpy as jnp
from jax import lax
from jax.sharding import PartitionSpec as P

SEND_CAP = 2


def mask_rows(factors, block_ranks):
    rank_width = factors.shape[2]
    row_index = lax.broadcasted_iota(jnp.int32, (factors.shape[0], rank_width), 1)
    row_mask = row_index < block_ranks[:, None]
    return jnp.where(row_mask[:, None, :, None], factors, jnp.zeros((), factors.dtype))


def product(left, right):
    return jnp.einsum("prb,psb->prs", left, right, preferred_element_type=jnp.float32)


def gather_inverses(lower_rows, upper_rows):
    groups = lax.axis_size("x") * lax.axis_size("y")
    rows = lower_rows.shape[1]
    width = lower_rows.shape[2]
    span = width + rows
    start = (lax.axis_index("x") * lax.axis_size("y") + lax.axis_index("y")) * rows
    both = jnp.concatenate([upper_rows, lower_rows], axis=-1)
    packed = lax.dynamic_slice_in_dim(both, start, span, axis=2)
    near = lax.axis_size("y")
    copies = jnp.broadcast_to(packed[None], (near,) + packed.shape)
    blocks = lax.all_to_all(copies, "y", split_axis=0, concat_axis=0, tiled=True)
    copies = jnp.broadcast_to(blocks[None], (groups // near,) + blocks.shape)
    blocks = lax.all_to_all(copies, "x", split_axis=0, concat_axis=0, tiled=True)
    blocks = blocks.reshape((groups,) + packed.shape)
    upper_blocks, lower_blocks = [], []
    for source in range(groups):
        block = blocks[source]
        cut = width - source * rows
        upper_blocks.append(jnp.pad(block[..., :cut], ((0, 0), (0, 0), (source * rows, 0))))
        lower_blocks.append(jnp.pad(block[..., cut:], ((0, 0), (0, 0), (0, cut - rows))))
    return jnp.concatenate(lower_blocks, axis=1), jnp.concatenate(upper_blocks, axis=1)


def per_device(
    lower_inverse,
    upper_inverse,
    lower_factors,
    upper_factors,
    lower_ranks,
    upper_ranks,
    pivots,
    pair_lower,
    pair_upper,
    pair_owner,
):
    lower_masked = mask_rows(lower_factors[0], lower_ranks[0])
    upper_masked = mask_rows(upper_factors[0], upper_ranks[0])
    upper_pivoted = jnp.take(upper_masked, pivots[0], axis=3)
    block_count = lower_masked.shape[0]
    rank_width = lower_masked.shape[2]
    panel_count = lower_masked.shape[3]
    lower_real = lower_masked[:, 0].reshape(block_count * rank_width, panel_count)
    lower_imag = lower_masked[:, 1].reshape(block_count * rank_width, panel_count)
    upper_real = upper_pivoted[:, 0].reshape(block_count * rank_width, panel_count)
    upper_imag = upper_pivoted[:, 1].reshape(block_count * rank_width, panel_count)
    contract_last = (((1,), (1,)), ((), ()))
    lower_piece, upper_piece = gather_inverses(lower_inverse[0], upper_inverse[0])
    piece_real = upper_piece[0]
    piece_imag = upper_piece[1]
    real_part = jnp.dot(lower_real, piece_real, preferred_element_type=jnp.float32) - jnp.dot(
        lower_imag, piece_imag, preferred_element_type=jnp.float32
    )
    imag_part = jnp.dot(lower_real, piece_imag, preferred_element_type=jnp.float32) + jnp.dot(
        lower_imag, piece_real, preferred_element_type=jnp.float32
    )
    lower_totals = jnp.stack([real_part, imag_part], 0)
    piece_real = lower_piece[0]
    piece_imag = lower_piece[1]
    real_part = lax.dot_general(
        upper_real, piece_real, contract_last, preferred_element_type=jnp.float32
    ) - lax.dot_general(upper_imag, piece_imag, contract_last, preferred_element_type=jnp.float32)
    imag_part = lax.dot_general(
        upper_real, piece_imag, contract_last, preferred_element_type=jnp.float32
    ) + lax.dot_general(upper_imag, piece_real, contract_last, preferred_element_type=jnp.float32)
    upper_totals = jnp.stack([real_part, imag_part], 0)
    lower_totals = lower_totals.astype(jnp.bfloat16)
    upper_totals = upper_totals.astype(jnp.bfloat16)
    lower_solved = jnp.transpose(
        lower_totals.reshape(2, block_count, rank_width, panel_count), (1, 0, 2, 3)
    )
    upper_solved = jnp.transpose(
        upper_totals.reshape(2, block_count, rank_width, panel_count), (1, 0, 2, 3)
    )
    real_part = lax.dot_general(
        lower_totals[0], upper_totals[0], contract_last, preferred_element_type=jnp.float32
    ) - lax.dot_general(lower_totals[1], upper_totals[1], contract_last, preferred_element_type=jnp.float32)
    imag_part = lax.dot_general(
        lower_totals[0], upper_totals[1], contract_last, preferred_element_type=jnp.float32
    ) + lax.dot_general(lower_totals[1], upper_totals[0], contract_last, preferred_element_type=jnp.float32)
    grid = jnp.stack([real_part, imag_part], 0).reshape(2, block_count, rank_width, block_count, rank_width)
    grid = jnp.transpose(grid, (1, 3, 0, 2, 4)).reshape(
        block_count * block_count, 2, rank_width, rank_width
    )
    pair_count = pair_lower.shape[1]
    picked = jnp.take(grid, pair_lower[0] * block_count + pair_upper[0], axis=0)
    cores = picked.reshape(pair_count, 2 * rank_width * rank_width).astype(jnp.bfloat16)
    owners = pair_owner[0, :, 0]
    pair_ids = lax.broadcasted_iota(jnp.int32, (pair_count,), 0)
    same_owner = (owners[:, None] == owners[None, :]) & (pair_ids[None, :] < pair_ids[:, None])
    slots = jnp.sum(same_owner.astype(jnp.int32), axis=1)
    clusters = lax.axis_size("clu")
    target_slot = owners * SEND_CAP + slots
    slot_ids = lax.broadcasted_iota(jnp.int32, (clusters * SEND_CAP, pair_count), 0)
    one_hot = (slot_ids == target_slot[None, :]).astype(jnp.bfloat16)
    buffer = jnp.dot(one_hot, cores, preferred_element_type=jnp.float32).astype(jnp.bfloat16)
    buffer = buffer.reshape(clusters, SEND_CAP, 2, rank_width * rank_width)
    arrived = lax.all_to_all(buffer, "clu", split_axis=0, concat_axis=0, tiled=True)
    return (lower_solved[None], upper_solved[None], arrived[None, None])


def solution(mesh):
    grp_size = mesh.shape["grp"]
    near = 4 if grp_size % 4 == 0 else 1
    split_mesh = jax.sharding.Mesh(
        mesh.devices.reshape(grp_size // near, near, mesh.shape["clu"]), ("x", "y", "clu")
    )
    grp = ("x", "y")
    in_specs = (
        P("clu", None, grp, None),
        P("clu", None, grp, None),
        P("clu", grp, None, None, None),
        P("clu", grp, None, None, None),
        P("clu", grp),
        P("clu", grp),
        P("clu", None),
        P("clu", grp),
        P("clu", grp),
        P("clu", grp, None),
    )
    out_specs = (
        P("clu", grp, None, None, None),
        P("clu", grp, None, None, None),
        P("clu", grp, None, None, None, None),
    )
    return jax.shard_map(
        per_device, mesh=split_mesh, in_specs=in_specs, out_specs=out_specs, check_vma=False
    )
```

```python
import jax
import jax.numpy as jnp
from jax import lax
from jax.sharding import PartitionSpec as P

SEND_CAP = 2


def mask_rows(factors, block_ranks):
    rank_width = factors.shape[2]
    row_index = lax.broadcasted_iota(jnp.int32, (factors.shape[0], rank_width), 1)
    row_mask = row_index < block_ranks[:, None]
    return jnp.where(row_mask[:, None, :, None], factors, jnp.zeros((), factors.dtype))


def product(left, right):
    return jnp.einsum("prb,psb->prs", left, right, preferred_element_type=jnp.float32)


def gather_inverses(lower_rows, upper_rows):
    groups = lax.axis_size("grp")
    rows = lower_rows.shape[1]
    width = lower_rows.shape[2]
    span = width + rows
    start = lax.axis_index("grp") * rows
    both = jnp.concatenate([upper_rows, lower_rows], axis=-1)
    packed = lax.dynamic_slice_in_dim(both, start, span, axis=2)
    copies = jnp.broadcast_to(packed[None], (groups,) + packed.shape)
    blocks = lax.all_to_all(copies, "grp", split_axis=0, concat_axis=0, tiled=True)
    upper_blocks, lower_blocks = [], []
    for source in range(groups):
        block = blocks[source]
        cut = width - source * rows
        upper_blocks.append(jnp.pad(block[..., :cut], ((0, 0), (0, 0), (source * rows, 0))))
        lower_blocks.append(jnp.pad(block[..., cut:], ((0, 0), (0, 0), (0, cut - rows))))
    return jnp.concatenate(lower_blocks, axis=1), jnp.concatenate(upper_blocks, axis=1)


def per_device(
    lower_inverse,
    upper_inverse,
    lower_factors,
    upper_factors,
    lower_ranks,
    upper_ranks,
    pivots,
    pair_lower,
    pair_upper,
    pair_owner,
):
    lower_masked = mask_rows(lower_factors[0], lower_ranks[0])
    upper_masked = mask_rows(upper_factors[0], upper_ranks[0])
    upper_pivoted = jnp.take(upper_masked, pivots[0], axis=3)
    block_count = lower_masked.shape[0]
    rank_width = lower_masked.shape[2]
    panel_count = lower_masked.shape[3]
    lower_real = lower_masked[:, 0].reshape(block_count * rank_width, panel_count)
    lower_imag = lower_masked[:, 1].reshape(block_count * rank_width, panel_count)
    upper_real = upper_pivoted[:, 0].reshape(block_count * rank_width, panel_count)
    upper_imag = upper_pivoted[:, 1].reshape(block_count * rank_width, panel_count)
    contract_last = (((1,), (1,)), ((), ()))
    lower_piece, upper_piece = gather_inverses(lower_inverse[0], upper_inverse[0])
    piece_real = upper_piece[0]
    piece_imag = upper_piece[1]
    real_part = jnp.dot(lower_real, piece_real, preferred_element_type=jnp.float32) - jnp.dot(
        lower_imag, piece_imag, preferred_element_type=jnp.float32
    )
    imag_part = jnp.dot(lower_real, piece_imag, preferred_element_type=jnp.float32) + jnp.dot(
        lower_imag, piece_real, preferred_element_type=jnp.float32
    )
    lower_totals = jnp.stack([real_part, imag_part], 0)
    piece_real = lower_piece[0]
    piece_imag = lower_piece[1]
    real_part = lax.dot_general(
        upper_real, piece_real, contract_last, preferred_element_type=jnp.float32
    ) - lax.dot_general(upper_imag, piece_imag, contract_last, preferred_element_type=jnp.float32)
    imag_part = lax.dot_general(
        upper_real, piece_imag, contract_last, preferred_element_type=jnp.float32
    ) + lax.dot_general(upper_imag, piece_real, contract_last, preferred_element_type=jnp.float32)
    upper_totals = jnp.stack([real_part, imag_part], 0)
    lower_totals = lower_totals.astype(jnp.bfloat16)
    upper_totals = upper_totals.astype(jnp.bfloat16)
    lower_solved = jnp.transpose(
        lower_totals.reshape(2, block_count, rank_width, panel_count), (1, 0, 2, 3)
    )
    upper_solved = jnp.transpose(
        upper_totals.reshape(2, block_count, rank_width, panel_count), (1, 0, 2, 3)
    )
    real_part = lax.dot_general(
        lower_totals[0], upper_totals[0], contract_last, preferred_element_type=jnp.float32
    ) - lax.dot_general(lower_totals[1], upper_totals[1], contract_last, preferred_element_type=jnp.float32)
    imag_part = lax.dot_general(
        lower_totals[0], upper_totals[1], contract_last, preferred_element_type=jnp.float32
    ) + lax.dot_general(lower_totals[1], upper_totals[0], contract_last, preferred_element_type=jnp.float32)
    pair_count = pair_lower.shape[1]
    picked = [
        part.reshape(block_count, rank_width, block_count, rank_width)[pair_lower[0], :, pair_upper[0], :]
        for part in (real_part, imag_part)
    ]
    picked = jnp.stack(picked, 1)
    cores = picked.reshape(pair_count, 2 * rank_width * rank_width).astype(jnp.bfloat16)
    owners = pair_owner[0, :, 0]
    pair_ids = lax.broadcasted_iota(jnp.int32, (pair_count,), 0)
    same_owner = (owners[:, None] == owners[None, :]) & (pair_ids[None, :] < pair_ids[:, None])
    slots = jnp.sum(same_owner.astype(jnp.int32), axis=1)
    clusters = lax.axis_size("clu")
    target_slot = owners * SEND_CAP + slots
    slot_ids = lax.broadcasted_iota(jnp.int32, (clusters * SEND_CAP, pair_count), 0)
    one_hot = (slot_ids == target_slot[None, :]).astype(jnp.bfloat16)
    buffer = jnp.dot(one_hot, cores, preferred_element_type=jnp.float32).astype(jnp.bfloat16)
    buffer = buffer.reshape(clusters, SEND_CAP, 2, rank_width * rank_width)
    arrived = lax.all_to_all(buffer, "clu", split_axis=0, concat_axis=0, tiled=True)
    return (lower_solved[None], upper_solved[None], arrived[None, None])


def solution(mesh):
    in_specs = (
        P("clu", None, "grp", None),
        P("clu", None, "grp", None),
        P("clu", "grp", None, None, None),
        P("clu", "grp", None, None, None),
        P("clu", "grp"),
        P("clu", "grp"),
        P("clu", None),
        P("clu", "grp"),
        P("clu", "grp"),
        P("clu", "grp", None),
    )
    out_specs = (
        P("clu", "grp", None, None, None),
        P("clu", "grp", None, None, None),
        P("clu", "grp", None, None, None, None),
    )
    return jax.shard_map(
        per_device, mesh=mesh, in_specs=in_specs, out_specs=out_specs, check_vma=False
    )
```

```python
import jax
import jax.numpy as jnp
from jax import lax
from jax.sharding import PartitionSpec as P

SEND_CAP = 2


def mask_rows(factors, block_ranks):
    rank_width = factors.shape[2]
    row_index = lax.broadcasted_iota(jnp.int32, (factors.shape[0], rank_width), 1)
    row_mask = row_index < block_ranks[:, None]
    return jnp.where(row_mask[:, None, :, None], factors, jnp.zeros((), factors.dtype))


def product(left, right):
    return jnp.einsum("prb,psb->prs", left, right, preferred_element_type=jnp.float32)


def gather_inverses(lower_rows, upper_rows):
    groups = lax.axis_size("grp")
    rows = lower_rows.shape[1]
    width = lower_rows.shape[2]
    span = width + rows
    start = lax.axis_index("grp") * rows
    both = jnp.concatenate([upper_rows, lower_rows], axis=-1)
    packed = lax.dynamic_slice_in_dim(both, start, span, axis=2)
    copies = jnp.broadcast_to(packed[None], (groups,) + packed.shape)
    blocks = lax.all_to_all(copies, "grp", split_axis=0, concat_axis=0, tiled=True)
    upper_blocks, lower_blocks = [], []
    for source in range(groups):
        block = blocks[source]
        cut = width - source * rows
        upper_blocks.append(jnp.pad(block[..., :cut], ((0, 0), (0, 0), (source * rows, 0))))
        lower_blocks.append(jnp.pad(block[..., cut:], ((0, 0), (0, 0), (0, cut - rows))))
    return jnp.concatenate(lower_blocks, axis=1), jnp.concatenate(upper_blocks, axis=1)


def per_device(
    lower_inverse,
    upper_inverse,
    lower_factors,
    upper_factors,
    lower_ranks,
    upper_ranks,
    pivots,
    pair_lower,
    pair_upper,
    pair_owner,
):
    lower_masked = mask_rows(lower_factors[0], lower_ranks[0])
    upper_masked = mask_rows(upper_factors[0], upper_ranks[0])
    upper_pivoted = jnp.take(upper_masked, pivots[0], axis=3)
    block_count = lower_masked.shape[0]
    rank_width = lower_masked.shape[2]
    panel_count = lower_masked.shape[3]
    lower_real = lower_masked[:, 0].reshape(block_count * rank_width, panel_count)
    lower_imag = lower_masked[:, 1].reshape(block_count * rank_width, panel_count)
    upper_real = upper_pivoted[:, 0].reshape(block_count * rank_width, panel_count)
    upper_imag = upper_pivoted[:, 1].reshape(block_count * rank_width, panel_count)
    contract_last = (((1,), (1,)), ((), ()))
    lower_piece, upper_piece = gather_inverses(lower_inverse[0], upper_inverse[0])
    piece_real = upper_piece[0]
    piece_imag = upper_piece[1]
    real_part = jnp.dot(lower_real, piece_real, preferred_element_type=jnp.float32) - jnp.dot(
        lower_imag, piece_imag, preferred_element_type=jnp.float32
    )
    imag_part = jnp.dot(lower_real, piece_imag, preferred_element_type=jnp.float32) + jnp.dot(
        lower_imag, piece_real, preferred_element_type=jnp.float32
    )
    lower_totals = jnp.stack([real_part, imag_part], 0)
    piece_real = lower_piece[0]
    piece_imag = lower_piece[1]
    real_part = lax.dot_general(
        upper_real, piece_real, contract_last, preferred_element_type=jnp.float32
    ) - lax.dot_general(upper_imag, piece_imag, contract_last, preferred_element_type=jnp.float32)
    imag_part = lax.dot_general(
        upper_real, piece_imag, contract_last, preferred_element_type=jnp.float32
    ) + lax.dot_general(upper_imag, piece_real, contract_last, preferred_element_type=jnp.float32)
    upper_totals = jnp.stack([real_part, imag_part], 0)
    lower_totals = lower_totals.astype(jnp.bfloat16)
    upper_totals = upper_totals.astype(jnp.bfloat16)
    lower_solved = jnp.transpose(
        lower_totals.reshape(2, block_count, rank_width, panel_count), (1, 0, 2, 3)
    )
    upper_solved = jnp.transpose(
        upper_totals.reshape(2, block_count, rank_width, panel_count), (1, 0, 2, 3)
    )
    real_part = lax.dot_general(
        lower_totals[0], upper_totals[0], contract_last, preferred_element_type=jnp.float32
    ) - lax.dot_general(lower_totals[1], upper_totals[1], contract_last, preferred_element_type=jnp.float32)
    imag_part = lax.dot_general(
        lower_totals[0], upper_totals[1], contract_last, preferred_element_type=jnp.float32
    ) + lax.dot_general(lower_totals[1], upper_totals[0], contract_last, preferred_element_type=jnp.float32)
    pair_count = pair_lower.shape[1]
    side = block_count * rank_width
    line_ids = lax.broadcasted_iota(jnp.int32, (pair_count, rank_width, side), 2)
    within = lax.broadcasted_iota(jnp.int32, (pair_count, rank_width, side), 1)
    row_pick = (line_ids == pair_lower[0][:, None, None] * rank_width + within).astype(jnp.bfloat16)
    col_pick = (line_ids == pair_upper[0][:, None, None] * rank_width + within).astype(jnp.bfloat16)
    picked = []
    for part in (real_part, imag_part):
        rows_of = jnp.dot(
            row_pick.reshape(pair_count * rank_width, side),
            part.astype(jnp.bfloat16),
            preferred_element_type=jnp.float32,
        ).astype(jnp.bfloat16).reshape(pair_count, rank_width, side)
        picked.append(
            jnp.einsum("qrl,qsl->qrs", rows_of, col_pick, preferred_element_type=jnp.float32)
        )
    picked = jnp.stack(picked, 1)
    cores = picked.reshape(pair_count, 2 * rank_width * rank_width).astype(jnp.bfloat16)
    owners = pair_owner[0, :, 0]
    pair_ids = lax.broadcasted_iota(jnp.int32, (pair_count,), 0)
    same_owner = (owners[:, None] == owners[None, :]) & (pair_ids[None, :] < pair_ids[:, None])
    slots = jnp.sum(same_owner.astype(jnp.int32), axis=1)
    clusters = lax.axis_size("clu")
    target_slot = owners * SEND_CAP + slots
    slot_ids = lax.broadcasted_iota(jnp.int32, (clusters * SEND_CAP, pair_count), 0)
    one_hot = (slot_ids == target_slot[None, :]).astype(jnp.bfloat16)
    buffer = jnp.dot(one_hot, cores, preferred_element_type=jnp.float32).astype(jnp.bfloat16)
    buffer = buffer.reshape(clusters, SEND_CAP, 2, rank_width * rank_width)
    arrived = lax.all_to_all(buffer, "clu", split_axis=0, concat_axis=0, tiled=True)
    return (lower_solved[None], upper_solved[None], arrived[None, None])


def solution(mesh):
    in_specs = (
        P("clu", None, "grp", None),
        P("clu", None, "grp", None),
        P("clu", "grp", None, None, None),
        P("clu", "grp", None, None, None),
        P("clu", "grp"),
        P("clu", "grp"),
        P("clu", None),
        P("clu", "grp"),
        P("clu", "grp"),
        P("clu", "grp", None),
    )
    out_specs = (
        P("clu", "grp", None, None, None),
        P("clu", "grp", None, None, None),
        P("clu", "grp", None, None, None, None),
    )
    return jax.shard_map(
        per_device, mesh=mesh, in_specs=in_specs, out_specs=out_specs, check_vma=False
    )
```

```python
import jax
import jax.numpy as jnp
from jax import lax
from jax.sharding import PartitionSpec as P

SEND_CAP = 2


def mask_rows(factors, block_ranks):
    rank_width = factors.shape[2]
    row_index = lax.broadcasted_iota(jnp.int32, (factors.shape[0], rank_width), 1)
    row_mask = row_index < block_ranks[:, None]
    return jnp.where(row_mask[:, None, :, None], factors, jnp.zeros((), factors.dtype))


def product(left, right):
    return jnp.einsum("prb,psb->prs", left, right, preferred_element_type=jnp.float32)


def gather_inverses(lower_rows, upper_rows):
    groups = lax.axis_size("grp")
    rows = lower_rows.shape[1]
    width = lower_rows.shape[2]
    span = width + rows
    start = lax.axis_index("grp") * rows
    both = jnp.concatenate([upper_rows, lower_rows], axis=-1)
    packed = lax.dynamic_slice_in_dim(both, start, span, axis=2)
    copies = jnp.broadcast_to(packed[None], (groups,) + packed.shape)
    blocks = lax.all_to_all(copies, "grp", split_axis=0, concat_axis=0, tiled=True)
    upper_blocks, lower_blocks = [], []
    for source in range(groups):
        block = blocks[source]
        cut = width - source * rows
        upper_blocks.append(jnp.pad(block[..., :cut], ((0, 0), (0, 0), (source * rows, 0))))
        lower_blocks.append(jnp.pad(block[..., cut:], ((0, 0), (0, 0), (0, cut - rows))))
    return jnp.concatenate(lower_blocks, axis=1), jnp.concatenate(upper_blocks, axis=1)


def per_device(
    lower_inverse,
    upper_inverse,
    lower_factors,
    upper_factors,
    lower_ranks,
    upper_ranks,
    pivots,
    pair_lower,
    pair_upper,
    pair_owner,
):
    lower_masked = mask_rows(lower_factors[0], lower_ranks[0])
    upper_masked = mask_rows(upper_factors[0], upper_ranks[0])
    upper_pivoted = jnp.take(upper_masked, pivots[0], axis=3)
    block_count = lower_masked.shape[0]
    rank_width = lower_masked.shape[2]
    panel_count = lower_masked.shape[3]
    lower_real = lower_masked[:, 0].reshape(block_count * rank_width, panel_count)
    lower_imag = lower_masked[:, 1].reshape(block_count * rank_width, panel_count)
    upper_real = upper_pivoted[:, 0].reshape(block_count * rank_width, panel_count)
    upper_imag = upper_pivoted[:, 1].reshape(block_count * rank_width, panel_count)
    contract_last = (((1,), (1,)), ((), ()))
    lower_piece, upper_piece = gather_inverses(lower_inverse[0], upper_inverse[0])
    piece_real = upper_piece[0]
    piece_imag = upper_piece[1]
    real_part = jnp.dot(lower_real, piece_real, preferred_element_type=jnp.float32) - jnp.dot(
        lower_imag, piece_imag, preferred_element_type=jnp.float32
    )
    imag_part = jnp.dot(lower_real, piece_imag, preferred_element_type=jnp.float32) + jnp.dot(
        lower_imag, piece_real, preferred_element_type=jnp.float32
    )
    lower_totals = jnp.stack([real_part, imag_part], 0)
    piece_real = lower_piece[0]
    piece_imag = lower_piece[1]
    real_part = lax.dot_general(
        upper_real, piece_real, contract_last, preferred_element_type=jnp.float32
    ) - lax.dot_general(upper_imag, piece_imag, contract_last, preferred_element_type=jnp.float32)
    imag_part = lax.dot_general(
        upper_real, piece_imag, contract_last, preferred_element_type=jnp.float32
    ) + lax.dot_general(upper_imag, piece_real, contract_last, preferred_element_type=jnp.float32)
    upper_totals = jnp.stack([real_part, imag_part], 0)
    lower_totals = lower_totals.astype(jnp.bfloat16)
    upper_totals = upper_totals.astype(jnp.bfloat16)
    lower_solved = jnp.transpose(
        lower_totals.reshape(2, block_count, rank_width, panel_count), (1, 0, 2, 3)
    )
    upper_solved = jnp.transpose(
        upper_totals.reshape(2, block_count, rank_width, panel_count), (1, 0, 2, 3)
    )
    lane_tile = 128
    padded = jnp.pad(
        upper_totals.reshape(2, block_count, rank_width, panel_count),
        ((0, 0), (0, 0), (0, lane_tile - rank_width), (0, 0)),
    ).reshape(2, block_count * lane_tile, panel_count)
    real_part = lax.dot_general(
        lower_totals[0], padded[0], contract_last, preferred_element_type=jnp.float32
    ) - lax.dot_general(lower_totals[1], padded[1], contract_last, preferred_element_type=jnp.float32)
    imag_part = lax.dot_general(
        lower_totals[0], padded[1], contract_last, preferred_element_type=jnp.float32
    ) + lax.dot_general(lower_totals[1], padded[0], contract_last, preferred_element_type=jnp.float32)
    grid = jnp.stack([real_part, imag_part], 0).reshape(2, block_count, rank_width, block_count, lane_tile)
    pair_count = pair_lower.shape[1]
    picked = grid[:, pair_lower[0], :, pair_upper[0], :][..., :rank_width]
    cores = picked.reshape(pair_count, 2 * rank_width * rank_width).astype(jnp.bfloat16)
    owners = pair_owner[0, :, 0]
    pair_ids = lax.broadcasted_iota(jnp.int32, (pair_count,), 0)
    same_owner = (owners[:, None] == owners[None, :]) & (pair_ids[None, :] < pair_ids[:, None])
    slots = jnp.sum(same_owner.astype(jnp.int32), axis=1)
    clusters = lax.axis_size("clu")
    target_slot = owners * SEND_CAP + slots
    slot_ids = lax.broadcasted_iota(jnp.int32, (clusters * SEND_CAP, pair_count), 0)
    one_hot = (slot_ids == target_slot[None, :]).astype(jnp.bfloat16)
    buffer = jnp.dot(one_hot, cores, preferred_element_type=jnp.float32).astype(jnp.bfloat16)
    buffer = buffer.reshape(clusters, SEND_CAP, 2, rank_width * rank_width)
    arrived = lax.all_to_all(buffer, "clu", split_axis=0, concat_axis=0, tiled=True)
    return (lower_solved[None], upper_solved[None], arrived[None, None])


def solution(mesh):
    in_specs = (
        P("clu", None, "grp", None),
        P("clu", None, "grp", None),
        P("clu", "grp", None, None, None),
        P("clu", "grp", None, None, None),
        P("clu", "grp"),
        P("clu", "grp"),
        P("clu", None),
        P("clu", "grp"),
        P("clu", "grp"),
        P("clu", "grp", None),
    )
    out_specs = (
        P("clu", "grp", None, None, None),
        P("clu", "grp", None, None, None),
        P("clu", "grp", None, None, None, None),
    )
    return jax.shard_map(
        per_device, mesh=mesh, in_specs=in_specs, out_specs=out_specs, check_vma=False
    )
```

```python
import jax
import jax.numpy as jnp
from jax import lax
from jax.sharding import PartitionSpec as P

SEND_CAP = 2


def mask_rows(factors, block_ranks):
    rank_width = factors.shape[2]
    row_index = lax.broadcasted_iota(jnp.int32, (factors.shape[0], rank_width), 1)
    row_mask = row_index < block_ranks[:, None]
    return jnp.where(row_mask[:, None, :, None], factors, jnp.zeros((), factors.dtype))


def product(left, right):
    return jnp.einsum("prb,psb->prs", left, right, preferred_element_type=jnp.float32)


def gather_inverses(lower_rows, upper_rows):
    groups = lax.axis_size("grp")
    rows = lower_rows.shape[1]
    width = lower_rows.shape[2]
    span = width + rows
    start = lax.axis_index("grp") * rows
    both = jnp.concatenate([upper_rows, lower_rows], axis=-1)
    packed = lax.dynamic_slice_in_dim(both, start, span, axis=2)
    copies = jnp.broadcast_to(packed[None], (groups,) + packed.shape)
    blocks = lax.all_to_all(copies, "grp", split_axis=0, concat_axis=0, tiled=True)
    upper_blocks, lower_blocks = [], []
    for source in range(groups):
        block = blocks[source]
        cut = width - source * rows
        upper_blocks.append(jnp.pad(block[..., :cut], ((0, 0), (0, 0), (source * rows, 0))))
        lower_blocks.append(jnp.pad(block[..., cut:], ((0, 0), (0, 0), (0, cut - rows))))
    return jnp.concatenate(lower_blocks, axis=1), jnp.concatenate(upper_blocks, axis=1)


def per_device(
    lower_inverse,
    upper_inverse,
    lower_factors,
    upper_factors,
    lower_ranks,
    upper_ranks,
    pivots,
    pair_lower,
    pair_upper,
    pair_owner,
):
    lower_masked = mask_rows(lower_factors[0], lower_ranks[0])
    upper_masked = mask_rows(upper_factors[0], upper_ranks[0])
    upper_pivoted = jnp.take(upper_masked, pivots[0], axis=3)
    block_count = lower_masked.shape[0]
    rank_width = lower_masked.shape[2]
    panel_count = lower_masked.shape[3]
    lower_real = lower_masked[:, 0].reshape(block_count * rank_width, panel_count)
    lower_imag = lower_masked[:, 1].reshape(block_count * rank_width, panel_count)
    upper_real = upper_pivoted[:, 0].reshape(block_count * rank_width, panel_count)
    upper_imag = upper_pivoted[:, 1].reshape(block_count * rank_width, panel_count)
    contract_last = (((1,), (1,)), ((), ()))
    lower_piece, upper_piece = gather_inverses(lower_inverse[0], upper_inverse[0])
    piece_real = upper_piece[0]
    piece_imag = upper_piece[1]
    real_part = jnp.dot(lower_real, piece_real, preferred_element_type=jnp.float32) - jnp.dot(
        lower_imag, piece_imag, preferred_element_type=jnp.float32
    )
    imag_part = jnp.dot(lower_real, piece_imag, preferred_element_type=jnp.float32) + jnp.dot(
        lower_imag, piece_real, preferred_element_type=jnp.float32
    )
    lower_totals = jnp.stack([real_part, imag_part], 0)
    piece_real = lower_piece[0]
    piece_imag = lower_piece[1]
    real_part = lax.dot_general(
        upper_real, piece_real, contract_last, preferred_element_type=jnp.float32
    ) - lax.dot_general(upper_imag, piece_imag, contract_last, preferred_element_type=jnp.float32)
    imag_part = lax.dot_general(
        upper_real, piece_imag, contract_last, preferred_element_type=jnp.float32
    ) + lax.dot_general(upper_imag, piece_real, contract_last, preferred_element_type=jnp.float32)
    upper_totals = jnp.stack([real_part, imag_part], 0)
    lower_totals = lower_totals.astype(jnp.bfloat16)
    upper_totals = upper_totals.astype(jnp.bfloat16)
    lower_solved = jnp.transpose(
        lower_totals.reshape(2, block_count, rank_width, panel_count), (1, 0, 2, 3)
    )
    upper_solved = jnp.transpose(
        upper_totals.reshape(2, block_count, rank_width, panel_count), (1, 0, 2, 3)
    )
    lane_tile = 128
    padded = jnp.pad(
        upper_totals.reshape(2, block_count, rank_width, panel_count),
        ((0, 0), (0, 0), (0, lane_tile - rank_width), (0, 0)),
    ).reshape(2, block_count * lane_tile, panel_count)
    real_part = lax.dot_general(
        lower_totals[0], padded[0], contract_last, preferred_element_type=jnp.float32
    ) - lax.dot_general(lower_totals[1], padded[1], contract_last, preferred_element_type=jnp.float32)
    imag_part = lax.dot_general(
        lower_totals[0], padded[1], contract_last, preferred_element_type=jnp.float32
    ) + lax.dot_general(lower_totals[1], padded[0], contract_last, preferred_element_type=jnp.float32)
    grid = jnp.stack([real_part, imag_part], 0).reshape(2, block_count, rank_width, block_count, lane_tile)
    pair_count = pair_lower.shape[1]
    picked = grid[:, pair_lower[0], :, pair_upper[0], :][..., :rank_width]
    cores = picked.reshape(pair_count, 2, rank_width * rank_width).astype(jnp.bfloat16)
    owners = pair_owner[0, :, 0]
    pair_ids = lax.broadcasted_iota(jnp.int32, (pair_count,), 0)
    same_owner = (owners[:, None] == owners[None, :]) & (pair_ids[None, :] < pair_ids[:, None])
    slots = jnp.sum(same_owner.astype(jnp.int32), axis=1)
    clusters = lax.axis_size("clu")
    target_slot = owners * SEND_CAP + slots
    slot_ids = lax.broadcasted_iota(jnp.int32, (clusters * SEND_CAP, pair_count), 0)
    filled = slot_ids == target_slot[None, :]
    source = jnp.where(
        jnp.any(filled, axis=1), jnp.argmax(filled, axis=1).astype(jnp.int32), pair_count
    )
    cores = jnp.concatenate([cores, jnp.zeros((1,) + cores.shape[1:], cores.dtype)], axis=0)
    buffer = jnp.take(cores, source, axis=0)
    buffer = buffer.reshape(clusters, SEND_CAP, 2, rank_width * rank_width)
    arrived = lax.all_to_all(buffer, "clu", split_axis=0, concat_axis=0, tiled=True)
    return (lower_solved[None], upper_solved[None], arrived[None, None])


def solution(mesh):
    in_specs = (
        P("clu", None, "grp", None),
        P("clu", None, "grp", None),
        P("clu", "grp", None, None, None),
        P("clu", "grp", None, None, None),
        P("clu", "grp"),
        P("clu", "grp"),
        P("clu", None),
        P("clu", "grp"),
        P("clu", "grp"),
        P("clu", "grp", None),
    )
    out_specs = (
        P("clu", "grp", None, None, None),
        P("clu", "grp", None, None, None),
        P("clu", "grp", None, None, None, None),
    )
    return jax.shard_map(
        per_device, mesh=mesh, in_specs=in_specs, out_specs=out_specs, check_vma=False
    )
```

```python
import jax
import jax.numpy as jnp
from jax import lax
from jax.sharding import PartitionSpec as P

SEND_CAP = 2


def mask_rows(factors, block_ranks):
    rank_width = factors.shape[2]
    row_index = lax.broadcasted_iota(jnp.int32, (factors.shape[0], rank_width), 1)
    row_mask = row_index < block_ranks[:, None]
    return jnp.where(row_mask[:, None, :, None], factors, jnp.zeros((), factors.dtype))


def product(left, right):
    return jnp.einsum("prb,psb->prs", left, right, preferred_element_type=jnp.float32)


def combine(by_real, by_imag):
    half = by_real.shape[0] // 2
    return jnp.stack([by_real[:half] - by_imag[half:], by_imag[:half] + by_real[half:]], 0)


def gather_inverses(lower_rows, upper_rows):
    groups = lax.axis_size("grp")
    rows = lower_rows.shape[1]
    width = lower_rows.shape[2]
    span = width + rows
    start = lax.axis_index("grp") * rows
    both = jnp.concatenate([upper_rows, lower_rows], axis=-1)
    packed = lax.dynamic_slice_in_dim(both, start, span, axis=2)
    copies = jnp.broadcast_to(packed[None], (groups,) + packed.shape)
    blocks = lax.all_to_all(copies, "grp", split_axis=0, concat_axis=0, tiled=True)
    upper_blocks, lower_blocks = [], []
    for source in range(groups):
        block = blocks[source]
        cut = width - source * rows
        upper_blocks.append(jnp.pad(block[..., :cut], ((0, 0), (0, 0), (source * rows, 0))))
        lower_blocks.append(jnp.pad(block[..., cut:], ((0, 0), (0, 0), (0, cut - rows))))
    return jnp.concatenate(lower_blocks, axis=1), jnp.concatenate(upper_blocks, axis=1)


def per_device(
    lower_inverse,
    upper_inverse,
    lower_factors,
    upper_factors,
    lower_ranks,
    upper_ranks,
    pivots,
    pair_lower,
    pair_upper,
    pair_owner,
):
    lower_masked = mask_rows(lower_factors[0], lower_ranks[0])
    upper_masked = mask_rows(upper_factors[0], upper_ranks[0])
    upper_pivoted = jnp.take(upper_masked, pivots[0], axis=3)
    block_count = lower_masked.shape[0]
    rank_width = lower_masked.shape[2]
    panel_count = lower_masked.shape[3]
    lower_rows = jnp.concatenate(
        [lower_masked[:, 0].reshape(block_count * rank_width, panel_count),
         lower_masked[:, 1].reshape(block_count * rank_width, panel_count)], axis=0)
    upper_rows = jnp.concatenate(
        [upper_pivoted[:, 0].reshape(block_count * rank_width, panel_count),
         upper_pivoted[:, 1].reshape(block_count * rank_width, panel_count)], axis=0)
    contract_last = (((1,), (1,)), ((), ()))
    lower_piece, upper_piece = gather_inverses(lower_inverse[0], upper_inverse[0])
    lower_totals = combine(
        jnp.dot(lower_rows, upper_piece[0], preferred_element_type=jnp.float32),
        jnp.dot(lower_rows, upper_piece[1], preferred_element_type=jnp.float32),
    )
    upper_totals = combine(
        lax.dot_general(upper_rows, lower_piece[0], contract_last, preferred_element_type=jnp.float32),
        lax.dot_general(upper_rows, lower_piece[1], contract_last, preferred_element_type=jnp.float32),
    )
    lower_totals = lower_totals.astype(jnp.bfloat16)
    upper_totals = upper_totals.astype(jnp.bfloat16)
    lower_solved = jnp.transpose(
        lower_totals.reshape(2, block_count, rank_width, panel_count), (1, 0, 2, 3)
    )
    upper_solved = jnp.transpose(
        upper_totals.reshape(2, block_count, rank_width, panel_count), (1, 0, 2, 3)
    )
    lane_tile = 128
    padded = jnp.pad(
        upper_totals.reshape(2, block_count, rank_width, panel_count),
        ((0, 0), (0, 0), (0, lane_tile - rank_width), (0, 0)),
    ).reshape(2, block_count * lane_tile, panel_count)
    both_rows = lower_totals.reshape(2 * block_count * rank_width, panel_count)
    real_part, imag_part = combine(
        lax.dot_general(both_rows, padded[0], contract_last, preferred_element_type=jnp.float32),
        lax.dot_general(both_rows, padded[1], contract_last, preferred_element_type=jnp.float32),
    )
    grid = jnp.stack([real_part, imag_part], 0).reshape(2, block_count, rank_width, block_count, lane_tile)
    pair_count = pair_lower.shape[1]
    picked = grid[:, pair_lower[0], :, pair_upper[0], :][..., :rank_width]
    cores = picked.reshape(pair_count, 2 * rank_width * rank_width).astype(jnp.bfloat16)
    owners = pair_owner[0, :, 0]
    pair_ids = lax.broadcasted_iota(jnp.int32, (pair_count,), 0)
    same_owner = (owners[:, None] == owners[None, :]) & (pair_ids[None, :] < pair_ids[:, None])
    slots = jnp.sum(same_owner.astype(jnp.int32), axis=1)
    clusters = lax.axis_size("clu")
    target_slot = owners * SEND_CAP + slots
    slot_ids = lax.broadcasted_iota(jnp.int32, (clusters * SEND_CAP, pair_count), 0)
    one_hot = (slot_ids == target_slot[None, :]).astype(jnp.bfloat16)
    buffer = jnp.dot(one_hot, cores, preferred_element_type=jnp.float32).astype(jnp.bfloat16)
    buffer = buffer.reshape(clusters, SEND_CAP, 2, rank_width * rank_width)
    arrived = lax.all_to_all(buffer, "clu", split_axis=0, concat_axis=0, tiled=True)
    return (lower_solved[None], upper_solved[None], arrived[None, None])


def solution(mesh):
    in_specs = (
        P("clu", None, "grp", None),
        P("clu", None, "grp", None),
        P("clu", "grp", None, None, None),
        P("clu", "grp", None, None, None),
        P("clu", "grp"),
        P("clu", "grp"),
        P("clu", None),
        P("clu", "grp"),
        P("clu", "grp"),
        P("clu", "grp", None),
    )
    out_specs = (
        P("clu", "grp", None, None, None),
        P("clu", "grp", None, None, None),
        P("clu", "grp", None, None, None, None),
    )
    return jax.shard_map(
        per_device, mesh=mesh, in_specs=in_specs, out_specs=out_specs, check_vma=False
    )
```

```python
import jax
import jax.numpy as jnp
from jax import lax
from jax.sharding import PartitionSpec as P

SEND_CAP = 2


def mask_rows(factors, block_ranks):
    rank_width = factors.shape[2]
    row_index = lax.broadcasted_iota(jnp.int32, (factors.shape[0], rank_width), 1)
    row_mask = row_index < block_ranks[:, None]
    return jnp.where(row_mask[:, None, :, None], factors, jnp.zeros((), factors.dtype))


def product(left, right):
    return jnp.einsum("prb,psb->prs", left, right, preferred_element_type=jnp.float32)


def gather_inverses(lower_rows, upper_rows):
    groups = lax.axis_size("grp")
    rows = lower_rows.shape[1]
    width = lower_rows.shape[2]
    span = width + rows
    start = lax.axis_index("grp") * rows
    both = jnp.concatenate([upper_rows, lower_rows], axis=-1)
    packed = lax.dynamic_slice_in_dim(both, start, span, axis=2)
    copies = jnp.broadcast_to(packed[None], (groups,) + packed.shape)
    blocks = lax.all_to_all(copies, "grp", split_axis=0, concat_axis=0, tiled=True)
    both_rows = []
    for source in range(groups):
        offset = source * rows
        both_rows.append(jnp.pad(blocks[source], ((0, 0), (0, 0), (offset, 2 * width - span - offset))))
    both_full = jnp.concatenate(both_rows, axis=1)
    return both_full[..., width:], both_full[..., :width]

def per_device(
    lower_inverse,
    upper_inverse,
    lower_factors,
    upper_factors,
    lower_ranks,
    upper_ranks,
    pivots,
    pair_lower,
    pair_upper,
    pair_owner,
):
    lower_masked = mask_rows(lower_factors[0], lower_ranks[0])
    upper_masked = mask_rows(upper_factors[0], upper_ranks[0])
    upper_pivoted = jnp.take(upper_masked, pivots[0], axis=3)
    block_count = lower_masked.shape[0]
    rank_width = lower_masked.shape[2]
    panel_count = lower_masked.shape[3]
    lower_real = lower_masked[:, 0].reshape(block_count * rank_width, panel_count)
    lower_imag = lower_masked[:, 1].reshape(block_count * rank_width, panel_count)
    upper_real = upper_pivoted[:, 0].reshape(block_count * rank_width, panel_count)
    upper_imag = upper_pivoted[:, 1].reshape(block_count * rank_width, panel_count)
    contract_last = (((1,), (1,)), ((), ()))
    lower_piece, upper_piece = gather_inverses(lower_inverse[0], upper_inverse[0])
    piece_real = upper_piece[0]
    piece_imag = upper_piece[1]
    real_part = jnp.dot(lower_real, piece_real, preferred_element_type=jnp.float32) - jnp.dot(
        lower_imag, piece_imag, preferred_element_type=jnp.float32
    )
    imag_part = jnp.dot(lower_real, piece_imag, preferred_element_type=jnp.float32) + jnp.dot(
        lower_imag, piece_real, preferred_element_type=jnp.float32
    )
    lower_totals = jnp.stack([real_part, imag_part], 0)
    piece_real = lower_piece[0]
    piece_imag = lower_piece[1]
    real_part = lax.dot_general(
        upper_real, piece_real, contract_last, preferred_element_type=jnp.float32
    ) - lax.dot_general(upper_imag, piece_imag, contract_last, preferred_element_type=jnp.float32)
    imag_part = lax.dot_general(
        upper_real, piece_imag, contract_last, preferred_element_type=jnp.float32
    ) + lax.dot_general(upper_imag, piece_real, contract_last, preferred_element_type=jnp.float32)
    upper_totals = jnp.stack([real_part, imag_part], 0)
    lower_totals = lower_totals.astype(jnp.bfloat16)
    upper_totals = upper_totals.astype(jnp.bfloat16)
    lower_solved = jnp.transpose(
        lower_totals.reshape(2, block_count, rank_width, panel_count), (1, 0, 2, 3)
    )
    upper_solved = jnp.transpose(
        upper_totals.reshape(2, block_count, rank_width, panel_count), (1, 0, 2, 3)
    )
    lane_tile = 128
    padded = jnp.pad(
        upper_totals.reshape(2, block_count, rank_width, panel_count),
        ((0, 0), (0, 0), (0, lane_tile - rank_width), (0, 0)),
    ).reshape(2, block_count * lane_tile, panel_count)
    real_part = lax.dot_general(
        lower_totals[0], padded[0], contract_last, preferred_element_type=jnp.float32
    ) - lax.dot_general(lower_totals[1], padded[1], contract_last, preferred_element_type=jnp.float32)
    imag_part = lax.dot_general(
        lower_totals[0], padded[1], contract_last, preferred_element_type=jnp.float32
    ) + lax.dot_general(lower_totals[1], padded[0], contract_last, preferred_element_type=jnp.float32)
    grid = jnp.stack([real_part, imag_part], 0).reshape(2, block_count, rank_width, block_count, lane_tile)
    pair_count = pair_lower.shape[1]
    picked = grid[:, pair_lower[0], :, pair_upper[0], :][..., :rank_width]
    cores = picked.reshape(pair_count, 2 * rank_width * rank_width).astype(jnp.bfloat16)
    owners = pair_owner[0, :, 0]
    pair_ids = lax.broadcasted_iota(jnp.int32, (pair_count,), 0)
    same_owner = (owners[:, None] == owners[None, :]) & (pair_ids[None, :] < pair_ids[:, None])
    slots = jnp.sum(same_owner.astype(jnp.int32), axis=1)
    clusters = lax.axis_size("clu")
    target_slot = owners * SEND_CAP + slots
    slot_ids = lax.broadcasted_iota(jnp.int32, (clusters * SEND_CAP, pair_count), 0)
    one_hot = (slot_ids == target_slot[None, :]).astype(jnp.bfloat16)
    buffer = jnp.dot(one_hot, cores, preferred_element_type=jnp.float32).astype(jnp.bfloat16)
    buffer = buffer.reshape(clusters, SEND_CAP, 2, rank_width * rank_width)
    arrived = lax.all_to_all(buffer, "clu", split_axis=0, concat_axis=0, tiled=True)
    return (lower_solved[None], upper_solved[None], arrived[None, None])


def solution(mesh):
    in_specs = (
        P("clu", None, "grp", None),
        P("clu", None, "grp", None),
        P("clu", "grp", None, None, None),
        P("clu", "grp", None, None, None),
        P("clu", "grp"),
        P("clu", "grp"),
        P("clu", None),
        P("clu", "grp"),
        P("clu", "grp"),
        P("clu", "grp", None),
    )
    out_specs = (
        P("clu", "grp", None, None, None),
        P("clu", "grp", None, None, None),
        P("clu", "grp", None, None, None, None),
    )
    return jax.shard_map(
        per_device, mesh=mesh, in_specs=in_specs, out_specs=out_specs, check_vma=False
    )
```

```python
import jax
import jax.numpy as jnp
from jax import lax
from jax.sharding import PartitionSpec as P

SEND_CAP = 2


def mask_rows(factors, block_ranks):
    rank_width = factors.shape[2]
    row_index = lax.broadcasted_iota(jnp.int32, (factors.shape[0], rank_width), 1)
    row_mask = row_index < block_ranks[:, None]
    return jnp.where(row_mask[:, None, :, None], factors, jnp.zeros((), factors.dtype))


def product(left, right):
    return jnp.einsum("prb,psb->prs", left, right, preferred_element_type=jnp.float32)


def gather_inverses(lower_rows, upper_rows):
    groups = lax.axis_size("grp")
    rows = lower_rows.shape[1]
    width = lower_rows.shape[2]
    span = width + rows
    start = lax.axis_index("grp") * rows
    both = jnp.concatenate([upper_rows, lower_rows], axis=-1)
    packed = lax.dynamic_slice_in_dim(both, start, span, axis=2)
    copies = jnp.broadcast_to(packed[None], (groups,) + packed.shape)
    blocks = lax.all_to_all(copies, "grp", split_axis=0, concat_axis=0, tiled=True)
    both_rows = []
    for source in range(groups):
        offset = source * rows
        both_rows.append(jnp.pad(blocks[source], ((0, 0), (0, 0), (offset, 2 * width - span - offset))))
    both_full = jnp.concatenate(both_rows, axis=1)
    return both_full[..., width:], both_full[..., :width]

def per_device(
    lower_inverse,
    upper_inverse,
    lower_factors,
    upper_factors,
    lower_ranks,
    upper_ranks,
    pivots,
    pair_lower,
    pair_upper,
    pair_owner,
):
    lower_masked = mask_rows(lower_factors[0], lower_ranks[0])
    upper_masked = mask_rows(upper_factors[0], upper_ranks[0])
    upper_pivoted = jnp.take(upper_masked, pivots[0], axis=3)
    block_count = lower_masked.shape[0]
    rank_width = lower_masked.shape[2]
    panel_count = lower_masked.shape[3]
    lower_real = lower_masked[:, 0].reshape(block_count * rank_width, panel_count)
    lower_imag = lower_masked[:, 1].reshape(block_count * rank_width, panel_count)
    upper_real = upper_pivoted[:, 0].reshape(block_count * rank_width, panel_count)
    upper_imag = upper_pivoted[:, 1].reshape(block_count * rank_width, panel_count)
    contract_last = (((1,), (1,)), ((), ()))
    lower_piece, upper_piece = gather_inverses(lower_inverse[0], upper_inverse[0])
    piece_real = upper_piece[0]
    piece_imag = upper_piece[1]
    real_part = jnp.dot(lower_real, piece_real, preferred_element_type=jnp.float32) - jnp.dot(
        lower_imag, piece_imag, preferred_element_type=jnp.float32
    )
    imag_part = jnp.dot(lower_real, piece_imag, preferred_element_type=jnp.float32) + jnp.dot(
        lower_imag, piece_real, preferred_element_type=jnp.float32
    )
    lower_totals = jnp.stack([real_part, imag_part], 0)
    piece_real = lower_piece[0]
    piece_imag = lower_piece[1]
    real_part = lax.dot_general(
        upper_real, piece_real, contract_last, preferred_element_type=jnp.float32
    ) - lax.dot_general(upper_imag, piece_imag, contract_last, preferred_element_type=jnp.float32)
    imag_part = lax.dot_general(
        upper_real, piece_imag, contract_last, preferred_element_type=jnp.float32
    ) + lax.dot_general(upper_imag, piece_real, contract_last, preferred_element_type=jnp.float32)
    upper_totals = jnp.stack([real_part, imag_part], 0)
    lower_totals = lower_totals.astype(jnp.bfloat16)
    upper_totals = upper_totals.astype(jnp.bfloat16)
    lower_solved = jnp.transpose(
        lower_totals.reshape(2, block_count, rank_width, panel_count), (1, 0, 2, 3)
    )
    upper_solved = jnp.transpose(
        upper_totals.reshape(2, block_count, rank_width, panel_count), (1, 0, 2, 3)
    )
    lane_tile = 128
    padded = jnp.pad(
        upper_totals.reshape(2, block_count, rank_width, panel_count),
        ((0, 0), (0, 0), (0, lane_tile - rank_width), (0, 0)),
    ).reshape(2, block_count * lane_tile, panel_count)
    both_rows = lower_totals.reshape(2 * block_count * rank_width, panel_count)
    by_real = lax.dot_general(both_rows, padded[0], contract_last, preferred_element_type=jnp.float32)
    by_imag = lax.dot_general(both_rows, padded[1], contract_last, preferred_element_type=jnp.float32)
    half = block_count * rank_width
    real_part = by_real[:half] - by_imag[half:]
    imag_part = by_imag[:half] + by_real[half:]
    grid = jnp.stack([real_part, imag_part], 0).reshape(2, block_count, rank_width, block_count, lane_tile)
    pair_count = pair_lower.shape[1]
    picked = grid[:, pair_lower[0], :, pair_upper[0], :][..., :rank_width]
    cores = picked.reshape(pair_count, 2 * rank_width * rank_width).astype(jnp.bfloat16)
    owners = pair_owner[0, :, 0]
    pair_ids = lax.broadcasted_iota(jnp.int32, (pair_count,), 0)
    same_owner = (owners[:, None] == owners[None, :]) & (pair_ids[None, :] < pair_ids[:, None])
    slots = jnp.sum(same_owner.astype(jnp.int32), axis=1)
    clusters = lax.axis_size("clu")
    target_slot = owners * SEND_CAP + slots
    slot_ids = lax.broadcasted_iota(jnp.int32, (clusters * SEND_CAP, pair_count), 0)
    one_hot = (slot_ids == target_slot[None, :]).astype(jnp.bfloat16)
    buffer = jnp.dot(one_hot, cores, preferred_element_type=jnp.float32).astype(jnp.bfloat16)
    buffer = buffer.reshape(clusters, SEND_CAP, 2, rank_width * rank_width)
    arrived = lax.all_to_all(buffer, "clu", split_axis=0, concat_axis=0, tiled=True)
    return (lower_solved[None], upper_solved[None], arrived[None, None])


def solution(mesh):
    in_specs = (
        P("clu", None, "grp", None),
        P("clu", None, "grp", None),
        P("clu", "grp", None, None, None),
        P("clu", "grp", None, None, None),
        P("clu", "grp"),
        P("clu", "grp"),
        P("clu", None),
        P("clu", "grp"),
        P("clu", "grp"),
        P("clu", "grp", None),
    )
    out_specs = (
        P("clu", "grp", None, None, None),
        P("clu", "grp", None, None, None),
        P("clu", "grp", None, None, None, None),
    )
    return jax.shard_map(
        per_device, mesh=mesh, in_specs=in_specs, out_specs=out_specs, check_vma=False
    )
```
